256 devices in a mesh: gx: 32 (over z_hi, x, core), gy: 4 (over y), gz: 2 (over z_lo).
Axes of the slice: x: 4, y: 4, z: 8 (z_hi: 4, z_lo: 2; z = z_hi * 2 + z_lo), core: 2. Of those that a mesh axis runs over, the one named last changes fastest.
Arguments:
- unary: bfloat16 [128, 32, 128, 128], P('gx', 'gy', 'gz'), may hold values from -3 to 3
- compat: float32 [6, 128, 128], replicated, may hold values from -2.5 to 2.5
- saved_first: bfloat16 [6, 128, 32, 128, 128], P(None, 'gx', 'gy', 'gz'), may hold values from 0.25 to 4
- saved_second: bfloat16 [6, 128, 32, 128, 128], P(None, 'gx', 'gy', 'gz'), may hold values from 0.25 to 4
- cotangent: float32 [128, 32, 128, 128], P('gx', 'gy', 'gz'), may hold values from -6 to 6
Outputs:
- grad_unary: float32 [128, 32, 128, 128], P('gx', 'gy', 'gz')
- grad_compat: float32 [6, 128, 128], replicated
The draws below stay inside these ranges and needn't reach their ends.
All inputs are finite; a program needn't handle non-finite values.
Results may differ from the reference program's by a relative error of at most 0.0084.
Values may be sent and summed in bfloat16 or wider, within the bound.
No kernel may reach another device: no remote copies, remote signals or barrier semaphores. Data moves between devices by JAX's collectives and lax.ppermute only.
A program may use at most 128 MiB of HBM per device.

```python
import math
import jax
import jax.numpy as jnp
from jax import lax

L = 128
NX = 128
NY = 32
NZ = 128


def level_of(key, shape, cuts, low, top_value):
    loudness, own = 1.0, jax.random.fold_in(key, 6)
    for dim, parts in cuts:
        heights = jnp.exp(jax.random.uniform(jax.random.fold_in(own, dim), (parts,), jnp.float32, low / len(cuts), top_value / len(cuts)))
        loudness = loudness * jnp.repeat(heights, shape[dim] // parts).reshape([-1 if axis == dim else 1 for axis in range(len(shape))])
    return loudness


def scatter_about(stream_key, dims, width, reach, split=(), held_as=jnp.bfloat16):
    array = width * jax.random.normal(stream_key, dims, jnp.float32)
    if split:
        array = array * level_of(stream_key, dims, split, -0.22, 0.18)
    return jnp.clip(array, -reach, reach).astype(held_as)


def setup_inputs(seed: int = 0) -> dict:
    splits = jax.random.split(jax.random.key(seed), 6)
    unary = scatter_about(splits[0], (NX, NY, NZ, L), 1.0, 3.0, ((0, 32), (1, 4), (2, 2)))
    compat = scatter_about(splits[1], (6, L, L), 0.5, 2.5, (), jnp.float32)
    saved_first = jnp.clip(jnp.exp(math.log(4.0) - 2.7725887 * jax.random.uniform(splits[2], (6, NX, NY, NZ, L), jnp.float32) ** level_of(splits[2], (6, NX, NY, NZ, L), ((1, 32), (2, 4), (3, 2)), -0.2, 0.2)), 0.25, 4.0).astype(jnp.bfloat16)
    saved_second = jnp.clip(jnp.exp(math.log(4.0) - 2.7725887 * jax.random.uniform(splits[3], (6, NX, NY, NZ, L), jnp.float32) ** level_of(splits[3], (6, NX, NY, NZ, L), ((1, 32), (2, 4), (3, 2)), -0.2, 0.2)), 0.25, 4.0).astype(jnp.bfloat16)
    cotangent = scatter_about(splits[4], (NX, NY, NZ, L), 1.0, 6.0, ((0, 32), (1, 4), (2, 2)), jnp.float32)
    return dict(unary=unary, compat=compat, saved_first=saved_first, saved_second=saved_second, cotangent=cotangent)


OPPOSE = (1, 0, 3, 2, 5, 4)


def product_except(fields, skipped):
    result = None
    for index in range(6):
        if index in skipped:
            continue
        result = fields[index] if result is None else result * fields[index]
    return result


def send_terms(potential, messages, weights_b):
    labels = potential.shape[-1]
    hidden_b, normal, totals = [], [], []
    for direction in range(6):
        packed = (potential * product_except(messages, (OPPOSE[direction],))).astype(jnp.bfloat16)
        outgoing = jnp.dot(packed.reshape(-1, labels), weights_b[direction], preferred_element_type=jnp.float32).reshape(potential.shape)
        summed = jnp.sum(outgoing, axis=-1, keepdims=True)
        hidden_b.append(packed)
        normal.append(labels * outgoing / summed)
        totals.append(summed)
    return hidden_b, normal, totals


def forward_shift(normal_b):
    result = []
    for axis_dim in range(3):
        plus = normal_b[2 * axis_dim]
        minus = normal_b[2 * axis_dim + 1]
        length = plus.shape[axis_dim]
        ones = jnp.ones_like(lax.slice_in_dim(plus, 0, 1, axis=axis_dim))
        result.append(jnp.concatenate([ones, lax.slice_in_dim(plus, 0, length - 1, axis=axis_dim)], axis=axis_dim))
        result.append(jnp.concatenate([lax.slice_in_dim(minus, 1, length, axis=axis_dim), ones], axis=axis_dim))
    return result


def adjoint_shift(grad_b):
    result = []
    for axis_dim in range(3):
        plus = grad_b[2 * axis_dim]
        minus = grad_b[2 * axis_dim + 1]
        length = plus.shape[axis_dim]
        zeros = jnp.zeros_like(lax.slice_in_dim(plus, 0, 1, axis=axis_dim))
        result.append(jnp.concatenate([lax.slice_in_dim(plus, 1, length, axis=axis_dim), zeros], axis=axis_dim))
        result.append(jnp.concatenate([zeros, lax.slice_in_dim(minus, 0, length - 1, axis=axis_dim)], axis=axis_dim))
    return result


def belief_adjoint(potential, arriving, cotangent):
    labels = potential.shape[-1]
    whole = product_except(arriving, ())
    joint = potential * whole
    summed = jnp.sum(joint, axis=-1, keepdims=True)
    belief = joint / summed
    grad_joint = labels * (cotangent - jnp.sum(cotangent * belief, axis=-1, keepdims=True)) / summed
    grad_potential = grad_joint * whole
    grad_arriving = [(grad_joint * potential * product_except(arriving, (edge,))).astype(jnp.bfloat16) for edge in range(6)]
    return grad_arriving, grad_potential


def normal_adjoint(grad_normal, normal, totals):
    labels = normal.shape[-1]
    inner = jnp.sum(grad_normal * normal, axis=-1, keepdims=True)
    return ((labels / totals) * (grad_normal - inner / labels)).astype(jnp.bfloat16)


def local_adjoint(grad_normal, normal, totals, hidden_b, weights_b):
    labels = normal[0].shape[-1]
    grad_weights, grad_hidden = [], []
    for direction in range(6):
        grad_out = normal_adjoint(grad_normal[direction], normal[direction], totals[direction]).reshape(-1, labels)
        grad_weights.append(jnp.dot(hidden_b[direction].reshape(-1, labels).T, grad_out, preferred_element_type=jnp.float32))
        grad_hidden.append(jnp.dot(grad_out, weights_b[direction].T, preferred_element_type=jnp.float32).reshape(normal[0].shape))
    return jnp.stack(grad_weights), grad_hidden


def potential_terms(grad_hidden, messages):
    total = None
    for direction in range(6):
        term = grad_hidden[direction] * product_except(messages, (OPPOSE[direction],))
        total = term if total is None else total + term
    return total


def message_terms(grad_hidden, potential, messages):
    result = []
    for edge in range(6):
        total = None
        for direction in range(6):
            if direction == OPPOSE[edge]:
                continue
            term = grad_hidden[direction] * product_except(messages, (OPPOSE[direction], edge))
            total = term if total is None else total + term
        result.append((potential * total).astype(jnp.bfloat16))
    return result


def reference(unary, compat, saved_first, saved_second, cotangent):
    potential = jnp.exp(unary.astype(jnp.float32))
    weights = jnp.exp(compat)
    weights_b = weights.astype(jnp.bfloat16)
    first = [saved_first[index].astype(jnp.float32) for index in range(6)]
    second = [saved_second[index].astype(jnp.float32) for index in range(6)]
    hidden_two, normal_two, totals_two = send_terms(potential, second, weights_b)
    arriving = forward_shift([value.astype(jnp.bfloat16) for value in normal_two])
    arriving = [value.astype(jnp.float32) for value in arriving]
    grad_arriving, grad_potential = belief_adjoint(potential, arriving, cotangent)
    grad_normal_two = [value.astype(jnp.float32) for value in adjoint_shift(grad_arriving)]
    weights_two, grad_hidden_two = local_adjoint(grad_normal_two, normal_two, totals_two, hidden_two, weights_b)
    grad_potential = grad_potential + potential_terms(grad_hidden_two, second)
    grad_second = message_terms(grad_hidden_two, potential, second)
    hidden_one, normal_one, totals_one = send_terms(potential, first, weights_b)
    grad_normal_one = [value.astype(jnp.float32) for value in adjoint_shift(grad_second)]
    weights_one, grad_hidden_one = local_adjoint(grad_normal_one, normal_one, totals_one, hidden_one, weights_b)
    grad_potential = grad_potential + potential_terms(grad_hidden_one, first)
    grad_unary = potential * grad_potential
    grad_compat = weights * (weights_two + weights_one)
    return grad_unary, grad_compat
```

```python
import jax
import jax.numpy as jnp
from jax import lax
from jax.sharding import PartitionSpec as P

OPPOSE = (1, 0, 3, 2, 5, 4)


def extended(cells, sides, width):
    for axis, dim in sides:
        count = lax.axis_size(axis)
        ends = count - 1
        head = lax.slice_in_dim(cells, 0, width, axis=dim)
        tail = lax.slice_in_dim(cells, cells.shape[dim] - width, cells.shape[dim], axis=dim)
        cells = jnp.concatenate(
            [
                lax.ppermute(tail, axis, [(i, (i + 1) % count) for i in range(ends)]),
                cells,
                lax.ppermute(head, axis, [((i + 1) % count, i) for i in range(ends)]),
            ],
            axis=dim,
        )
    return cells


def full_product(fields):
    result = fields[0]
    for index in range(1, 6):
        result = result * fields[index]
    return result


def send_terms(potential, messages, whole, weights_b):
    labels = potential.shape[-1]
    scaled = potential * whole
    hidden = [scaled / messages[OPPOSE[direction]] for direction in range(6)]
    hidden_b = jnp.stack(hidden).astype(jnp.bfloat16)
    outgoing = jnp.einsum(
        "dxyzk,dkl->dxyzl", hidden_b, weights_b, preferred_element_type=jnp.float32
    )
    totals = jnp.sum(outgoing, axis=-1, keepdims=True)
    normal = labels * outgoing / totals
    return (hidden_b, normal, totals)


def trade(low_face, high_face, axis_dim):
    packed = jnp.concatenate([low_face, high_face], axis=axis_dim)
    if axis_dim == 0:
        rims = extended(packed, (("gx", 0),), 1)
    elif axis_dim == 1:
        rims = extended(packed, (("gy", 1),), 1)
    else:
        rims = extended(packed, (("gz", 2),), 1)
    lower = lax.slice_in_dim(rims, 0, 1, axis=axis_dim)
    upper = lax.slice_in_dim(rims, 3, 4, axis=axis_dim)
    return (lower, upper)


def spread(normal_b, lower_edge, upper_edge):
    result = []
    for axis_dim in range(3):
        plus = normal_b[2 * axis_dim]
        minus = normal_b[2 * axis_dim + 1]
        length = plus.shape[axis_dim]
        lower, upper = trade(
            lax.slice_in_dim(minus, 0, 1, axis=axis_dim),
            lax.slice_in_dim(plus, length - 1, length, axis=axis_dim),
            axis_dim,
        )
        ones = jnp.ones_like(lower)
        lower = jnp.where(lower_edge[axis_dim], ones, lower)
        upper = jnp.where(upper_edge[axis_dim], ones, upper)
        result.append(
            jnp.concatenate(
                [lower, lax.slice_in_dim(plus, 0, length - 1, axis=axis_dim)], axis=axis_dim
            )
        )
        result.append(
            jnp.concatenate(
                [lax.slice_in_dim(minus, 1, length, axis=axis_dim), upper], axis=axis_dim
            )
        )
    return result


def gather_back(grad_b):
    result = []
    for axis_dim in range(3):
        plus = grad_b[2 * axis_dim]
        minus = grad_b[2 * axis_dim + 1]
        length = plus.shape[axis_dim]
        lower, upper = trade(
            lax.slice_in_dim(plus, 0, 1, axis=axis_dim),
            lax.slice_in_dim(minus, length - 1, length, axis=axis_dim),
            axis_dim,
        )
        result.append(
            jnp.concatenate(
                [lax.slice_in_dim(plus, 1, length, axis=axis_dim), upper], axis=axis_dim
            )
        )
        result.append(
            jnp.concatenate(
                [lower, lax.slice_in_dim(minus, 0, length - 1, axis=axis_dim)], axis=axis_dim
            )
        )
    return jnp.stack(result).astype(jnp.float32)


def belief_adjoint(potential, arriving, cotangent):
    labels = potential.shape[-1]
    whole = full_product(arriving)
    joint = potential * whole
    summed = jnp.sum(joint, axis=-1, keepdims=True)
    belief = joint / summed
    grad_joint = labels * (cotangent - jnp.sum(cotangent * belief, axis=-1, keepdims=True)) / summed
    grad_potential = grad_joint * whole
    scaled = grad_joint * joint
    grad_arriving = [(scaled / arriving[edge]).astype(jnp.bfloat16) for edge in range(6)]
    return (grad_arriving, grad_potential)


def local_adjoint(grad_normal, normal, totals, hidden_b, weights_b):
    labels = normal.shape[-1]
    inner = jnp.sum(grad_normal * normal, axis=-1, keepdims=True)
    grad_out = (labels / totals * (grad_normal - inner / labels)).astype(jnp.bfloat16)
    grad_weights = jnp.einsum(
        "dxyzk,dxyzl->dkl", hidden_b, grad_out, preferred_element_type=jnp.float32
    )
    grad_hidden = jnp.einsum(
        "dxyzl,dkl->dxyzk", grad_out, weights_b, preferred_element_type=jnp.float32
    )
    return (grad_weights, grad_hidden)


def adjoint_terms(grad_hidden, potential, messages, whole):
    ratios = [grad_hidden[OPPOSE[index]] / messages[index] for index in range(6)]
    total = ratios[0]
    for index in range(1, 6):
        total = total + ratios[index]
    unary_term = whole * total
    scaled = potential * whole
    grad_messages = []
    for edge in range(6):
        partial_sum = None
        for index in range(6):
            if index == edge:
                continue
            partial_sum = ratios[index] if partial_sum is None else partial_sum + ratios[index]
        grad_messages.append((partial_sum * (scaled / messages[edge])).astype(jnp.bfloat16))
    return (unary_term, grad_messages)


def all_sum(value, axes):
    count = 1
    for axis in axes:
        count *= lax.axis_size(axis)
    rows = value.reshape(count, -1)
    mine = jnp.sum(lax.all_to_all(rows, axes, 0, 0, tiled=True), axis=0, keepdims=True)
    spread_out = jnp.broadcast_to(mine, rows.shape)
    return lax.all_to_all(spread_out, axes, 0, 0, tiled=True).reshape(value.shape)


def body(unary, compat, saved_first, saved_second, cotangent):
    potential = jnp.exp(unary.astype(jnp.float32))
    weights = jnp.exp(compat)
    weights_b = weights.astype(jnp.bfloat16)
    lower_edge = (lax.axis_index("gx") == 0, lax.axis_index("gy") == 0, lax.axis_index("gz") == 0)
    upper_edge = (
        lax.axis_index("gx") == lax.axis_size("gx") - 1,
        lax.axis_index("gy") == lax.axis_size("gy") - 1,
        lax.axis_index("gz") == lax.axis_size("gz") - 1,
    )
    first = [saved_first[index].astype(jnp.float32) for index in range(6)]
    second = [saved_second[index].astype(jnp.float32) for index in range(6)]
    whole_two = full_product(second)
    hidden_two, normal_two, totals_two = send_terms(potential, second, whole_two, weights_b)
    arriving = spread(
        [normal_two[index].astype(jnp.bfloat16) for index in range(6)], lower_edge, upper_edge
    )
    arriving = [value.astype(jnp.float32) for value in arriving]
    grad_arriving, grad_potential = belief_adjoint(potential, arriving, cotangent)
    grad_normal_two = gather_back(grad_arriving)
    weights_two, grad_hidden_two = local_adjoint(
        grad_normal_two, normal_two, totals_two, hidden_two, weights_b
    )
    unary_two, grad_second = adjoint_terms(grad_hidden_two, potential, second, whole_two)
    grad_potential = grad_potential + unary_two
    whole_one = full_product(first)
    hidden_one, normal_one, totals_one = send_terms(potential, first, whole_one, weights_b)
    grad_normal_one = gather_back(grad_second)
    weights_one, grad_hidden_one = local_adjoint(
        grad_normal_one, normal_one, totals_one, hidden_one, weights_b
    )
    ratios_one = [grad_hidden_one[OPPOSE[index]] / first[index] for index in range(6)]
    total_one = ratios_one[0]
    for index in range(1, 6):
        total_one = total_one + ratios_one[index]
    grad_potential = grad_potential + whole_one * total_one
    grad_unary = potential * grad_potential
    summed = all_sum(weights_two + weights_one, ("gx", "gy", "gz"))
    grad_compat = weights * summed
    return (grad_unary, grad_compat)


def solution(mesh):
    placed = (
        P("gx", "gy", "gz", None),
        P(),
        P(None, "gx", "gy", "gz", None),
        P(None, "gx", "gy", "gz", None),
        P("gx", "gy", "gz", None),
    )
    return jax.shard_map(
        body,
        mesh=mesh,
        in_specs=placed,
        out_specs=(P("gx", "gy", "gz", None), P()),
        check_vma=False,
    )
```

```python
import jax
import jax.numpy as jnp
from jax import lax
from jax.sharding import PartitionSpec as P

OPPOSE = (1, 0, 3, 2, 5, 4)


def extended(cells, sides, width):
    for axis, dim in sides:
        count = lax.axis_size(axis)
        ends = count - 1
        head = lax.slice_in_dim(cells, 0, width, axis=dim)
        tail = lax.slice_in_dim(cells, cells.shape[dim] - width, cells.shape[dim], axis=dim)
        cells = jnp.concatenate(
            [
                lax.ppermute(tail, axis, [(i, (i + 1) % count) for i in range(ends)]),
                cells,
                lax.ppermute(head, axis, [((i + 1) % count, i) for i in range(ends)]),
            ],
            axis=dim,
        )
    return cells


def full_product(fields):
    result = fields[0]
    for index in range(1, 6):
        result = result * fields[index]
    return result


def send_terms(potential, messages, whole, weights_b):
    labels = potential.shape[-1]
    scaled = potential * whole
    hidden = [scaled / messages[OPPOSE[direction]] for direction in range(6)]
    hidden_b = jnp.stack(hidden).astype(jnp.bfloat16)
    outgoing = jnp.einsum(
        "dxyzk,dkl->dxyzl", hidden_b, weights_b, preferred_element_type=jnp.float32
    )
    totals = jnp.sum(outgoing, axis=-1, keepdims=True)
    normal = labels * outgoing / totals
    return (hidden_b, normal, totals)


def trade(low_face, high_face, axis_dim):
    packed = jnp.concatenate([low_face, high_face], axis=axis_dim)
    if axis_dim == 0:
        rims = extended(packed, (("gx", 0),), 1)
    elif axis_dim == 1:
        rims = extended(packed, (("gy", 1),), 1)
    else:
        rims = extended(packed, (("gz", 2),), 1)
    lower = lax.slice_in_dim(rims, 0, 1, axis=axis_dim)
    upper = lax.slice_in_dim(rims, 3, 4, axis=axis_dim)
    return (lower, upper)


def spread(normal_b, lower_edge, upper_edge):
    result = []
    for axis_dim in range(3):
        plus = normal_b[2 * axis_dim]
        minus = normal_b[2 * axis_dim + 1]
        length = plus.shape[axis_dim]
        lower, upper = trade(
            lax.slice_in_dim(minus, 0, 1, axis=axis_dim),
            lax.slice_in_dim(plus, length - 1, length, axis=axis_dim),
            axis_dim,
        )
        ones = jnp.ones_like(lower)
        lower = jnp.where(lower_edge[axis_dim], ones, lower)
        upper = jnp.where(upper_edge[axis_dim], ones, upper)
        result.append(
            jnp.concatenate(
                [lower, lax.slice_in_dim(plus, 0, length - 1, axis=axis_dim)], axis=axis_dim
            )
        )
        result.append(
            jnp.concatenate(
                [lax.slice_in_dim(minus, 1, length, axis=axis_dim), upper], axis=axis_dim
            )
        )
    return result


def face_hidden(potential, messages, direction, axis_dim, index):
    layer = [lax.slice_in_dim(value, index, index + 1, axis=axis_dim) for value in messages]
    scaled = lax.slice_in_dim(potential, index, index + 1, axis=axis_dim) * full_product(layer)
    return (scaled / layer[OPPOSE[direction]]).astype(jnp.bfloat16)


def face_halos(potential, messages, weights_b):
    labels = potential.shape[-1]
    halos = []
    for axis_dim, axis in enumerate(("gx", "gy", "gz")):
        count = lax.axis_size(axis)
        length = potential.shape[axis_dim]
        for direction, index, pairs in (
            (2 * axis_dim, length - 1, [(i, i + 1) for i in range(count - 1)]),
            (2 * axis_dim + 1, 0, [(i + 1, i) for i in range(count - 1)]),
        ):
            hidden_b = face_hidden(potential, messages, direction, axis_dim, index)
            hidden_b = lax.ppermute(hidden_b, axis, pairs)
            outgoing = jnp.einsum(
                "xyzk,kl->xyzl", hidden_b, weights_b[direction], preferred_element_type=jnp.float32
            )
            totals = jnp.sum(outgoing, axis=-1, keepdims=True)
            halos.append((labels * outgoing / totals).astype(jnp.bfloat16))
    return halos


def spread_early(normal_b, halos, lower_edge, upper_edge):
    result = []
    for axis_dim in range(3):
        plus = normal_b[2 * axis_dim]
        minus = normal_b[2 * axis_dim + 1]
        length = plus.shape[axis_dim]
        lower = halos[2 * axis_dim]
        upper = halos[2 * axis_dim + 1]
        ones = jnp.ones_like(lower)
        lower = jnp.where(lower_edge[axis_dim], ones, lower)
        upper = jnp.where(upper_edge[axis_dim], ones, upper)
        result.append(
            jnp.concatenate(
                [lower, lax.slice_in_dim(plus, 0, length - 1, axis=axis_dim)], axis=axis_dim
            )
        )
        result.append(
            jnp.concatenate(
                [lax.slice_in_dim(minus, 1, length, axis=axis_dim), upper], axis=axis_dim
            )
        )
    return result


def gather_back(grad_b):
    result = []
    for axis_dim in range(3):
        plus = grad_b[2 * axis_dim]
        minus = grad_b[2 * axis_dim + 1]
        length = plus.shape[axis_dim]
        lower, upper = trade(
            lax.slice_in_dim(plus, 0, 1, axis=axis_dim),
            lax.slice_in_dim(minus, length - 1, length, axis=axis_dim),
            axis_dim,
        )
        result.append(
            jnp.concatenate(
                [lax.slice_in_dim(plus, 1, length, axis=axis_dim), upper], axis=axis_dim
            )
        )
        result.append(
            jnp.concatenate(
                [lower, lax.slice_in_dim(minus, 0, length - 1, axis=axis_dim)], axis=axis_dim
            )
        )
    return jnp.stack(result).astype(jnp.float32)


def belief_adjoint(potential, arriving, cotangent):
    labels = potential.shape[-1]
    whole = full_product(arriving)
    joint = potential * whole
    summed = jnp.sum(joint, axis=-1, keepdims=True)
    belief = joint / summed
    grad_joint = labels * (cotangent - jnp.sum(cotangent * belief, axis=-1, keepdims=True)) / summed
    grad_potential = grad_joint * whole
    scaled = grad_joint * joint
    grad_arriving = [(scaled / arriving[edge]).astype(jnp.bfloat16) for edge in range(6)]
    return (grad_arriving, grad_potential)


def local_adjoint(grad_normal, normal, totals, hidden_b, weights_b):
    labels = normal.shape[-1]
    inner = jnp.sum(grad_normal * normal, axis=-1, keepdims=True)
    grad_out = (labels / totals * (grad_normal - inner / labels)).astype(jnp.bfloat16)
    grad_weights = jnp.einsum(
        "dxyzk,dxyzl->dkl", hidden_b, grad_out, preferred_element_type=jnp.float32
    )
    grad_hidden = jnp.einsum(
        "dxyzl,dkl->dxyzk", grad_out, weights_b, preferred_element_type=jnp.float32
    )
    return (grad_weights, grad_hidden)


def adjoint_terms(grad_hidden, potential, messages, whole):
    ratios = [grad_hidden[OPPOSE[index]] / messages[index] for index in range(6)]
    total = ratios[0]
    for index in range(1, 6):
        total = total + ratios[index]
    unary_term = whole * total
    scaled = potential * whole
    grad_messages = []
    for edge in range(6):
        partial_sum = None
        for index in range(6):
            if index == edge:
                continue
            partial_sum = ratios[index] if partial_sum is None else partial_sum + ratios[index]
        grad_messages.append((partial_sum * (scaled / messages[edge])).astype(jnp.bfloat16))
    return (unary_term, grad_messages)


def all_sum(value, axes):
    count = 1
    for axis in axes:
        count *= lax.axis_size(axis)
    rows = value.reshape(count, -1)
    mine = jnp.sum(lax.all_to_all(rows, axes, 0, 0, tiled=True), axis=0, keepdims=True)
    spread_out = jnp.broadcast_to(mine, rows.shape)
    return lax.all_to_all(spread_out, axes, 0, 0, tiled=True).reshape(value.shape)


def body(unary, compat, saved_first, saved_second, cotangent):
    potential = jnp.exp(unary.astype(jnp.float32))
    weights = jnp.exp(compat)
    weights_b = weights.astype(jnp.bfloat16)
    lower_edge = (lax.axis_index("gx") == 0, lax.axis_index("gy") == 0, lax.axis_index("gz") == 0)
    upper_edge = (
        lax.axis_index("gx") == lax.axis_size("gx") - 1,
        lax.axis_index("gy") == lax.axis_size("gy") - 1,
        lax.axis_index("gz") == lax.axis_size("gz") - 1,
    )
    first = [saved_first[index].astype(jnp.float32) for index in range(6)]
    second = [saved_second[index].astype(jnp.float32) for index in range(6)]
    halos = face_halos(potential, second, weights_b)
    whole_two = full_product(second)
    hidden_two, normal_two, totals_two = send_terms(potential, second, whole_two, weights_b)
    arriving = spread_early(
        [normal_two[index].astype(jnp.bfloat16) for index in range(6)],
        halos,
        lower_edge,
        upper_edge,
    )
    arriving = [value.astype(jnp.float32) for value in arriving]
    grad_arriving, grad_potential = belief_adjoint(potential, arriving, cotangent)
    grad_normal_two = gather_back(grad_arriving)
    weights_two, grad_hidden_two = local_adjoint(
        grad_normal_two, normal_two, totals_two, hidden_two, weights_b
    )
    unary_two, grad_second = adjoint_terms(grad_hidden_two, potential, second, whole_two)
    grad_potential = grad_potential + unary_two
    whole_one = full_product(first)
    hidden_one, normal_one, totals_one = send_terms(potential, first, whole_one, weights_b)
    grad_normal_one = gather_back(grad_second)
    weights_one, grad_hidden_one = local_adjoint(
        grad_normal_one, normal_one, totals_one, hidden_one, weights_b
    )
    ratios_one = [grad_hidden_one[OPPOSE[index]] / first[index] for index in range(6)]
    total_one = ratios_one[0]
    for index in range(1, 6):
        total_one = total_one + ratios_one[index]
    grad_potential = grad_potential + whole_one * total_one
    grad_unary = potential * grad_potential
    summed = all_sum(weights_two + weights_one, ("gx", "gy", "gz"))
    grad_compat = weights * summed
    return (grad_unary, grad_compat)


def solution(mesh):
    placed = (
        P("gx", "gy", "gz", None),
        P(),
        P(None, "gx", "gy", "gz", None),
        P(None, "gx", "gy", "gz", None),
        P("gx", "gy", "gz", None),
    )
    return jax.shard_map(
        body,
        mesh=mesh,
        in_specs=placed,
        out_specs=(P("gx", "gy", "gz", None), P()),
        check_vma=False,
    )
```

```python
import jax
import jax.numpy as jnp
from jax import lax
from jax.sharding import PartitionSpec as P

OPPOSE = (1, 0, 3, 2, 5, 4)


def extended(cells, sides, width):
    for axis, dim in sides:
        count = lax.axis_size(axis)
        ends = count - 1
        head = lax.slice_in_dim(cells, 0, width, axis=dim)
        tail = lax.slice_in_dim(cells, cells.shape[dim] - width, cells.shape[dim], axis=dim)
        cells = jnp.concatenate(
            [
                lax.ppermute(tail, axis, [(i, (i + 1) % count) for i in range(ends)]),
                cells,
                lax.ppermute(head, axis, [((i + 1) % count, i) for i in range(ends)]),
            ],
            axis=dim,
        )
    return cells


def full_product(fields):
    result = fields[0]
    for index in range(1, 6):
        result = result * fields[index]
    return result


def send_terms(potential, messages, whole, weights_b):
    labels = potential.shape[-1]
    scaled = potential * whole
    hidden = [scaled / messages[OPPOSE[direction]] for direction in range(6)]
    hidden_b = jnp.stack(hidden).astype(jnp.bfloat16)
    outgoing = jnp.einsum(
        "dxyzk,dkl->dxyzl", hidden_b, weights_b, preferred_element_type=jnp.float32
    )
    totals = jnp.sum(outgoing, axis=-1, keepdims=True)
    normal = labels * outgoing / totals
    return (hidden_b, normal, totals)


def trade(low_face, high_face, axis_dim):
    axis = ("gx", "gy", "gz")[axis_dim]
    count = lax.axis_size(axis)
    odd = lax.axis_index(axis) % 2 == 1
    first = lax.ppermute(
        jnp.where(odd, low_face, high_face), axis, [(i, i ^ 1) for i in range(count)]
    )
    if count > 2:
        second = lax.ppermute(
            jnp.where(odd, high_face, low_face),
            axis,
            [(i, i + 1 if i % 2 == 1 else i - 1) for i in range(1, count - 1)],
        )
    else:
        second = jnp.zeros_like(first)
    lower = jnp.where(odd, first, second)
    upper = jnp.where(odd, second, first)
    return (lower, upper)


def spread(normal_b, lower_edge, upper_edge):
    result = []
    for axis_dim in range(3):
        plus = normal_b[2 * axis_dim]
        minus = normal_b[2 * axis_dim + 1]
        length = plus.shape[axis_dim]
        lower, upper = trade(
            lax.slice_in_dim(minus, 0, 1, axis=axis_dim),
            lax.slice_in_dim(plus, length - 1, length, axis=axis_dim),
            axis_dim,
        )
        ones = jnp.ones_like(lower)
        lower = jnp.where(lower_edge[axis_dim], ones, lower)
        upper = jnp.where(upper_edge[axis_dim], ones, upper)
        result.append(
            jnp.concatenate(
                [lower, lax.slice_in_dim(plus, 0, length - 1, axis=axis_dim)], axis=axis_dim
            )
        )
        result.append(
            jnp.concatenate(
                [lax.slice_in_dim(minus, 1, length, axis=axis_dim), upper], axis=axis_dim
            )
        )
    return result


def gather_back(grad_b):
    result = []
    for axis_dim in range(3):
        plus = grad_b[2 * axis_dim]
        minus = grad_b[2 * axis_dim + 1]
        length = plus.shape[axis_dim]
        lower, upper = trade(
            lax.slice_in_dim(plus, 0, 1, axis=axis_dim),
            lax.slice_in_dim(minus, length - 1, length, axis=axis_dim),
            axis_dim,
        )
        result.append(
            jnp.concatenate(
                [lax.slice_in_dim(plus, 1, length, axis=axis_dim), upper], axis=axis_dim
            )
        )
        result.append(
            jnp.concatenate(
                [lower, lax.slice_in_dim(minus, 0, length - 1, axis=axis_dim)], axis=axis_dim
            )
        )
    return jnp.stack(result).astype(jnp.float32)


def belief_adjoint(potential, arriving, cotangent):
    labels = potential.shape[-1]
    whole = full_product(arriving)
    joint = potential * whole
    summed = jnp.sum(joint, axis=-1, keepdims=True)
    belief = joint / summed
    grad_joint = labels * (cotangent - jnp.sum(cotangent * belief, axis=-1, keepdims=True)) / summed
    grad_potential = grad_joint * whole
    scaled = grad_joint * joint
    grad_arriving = [(scaled / arriving[edge]).astype(jnp.bfloat16) for edge in range(6)]
    return (grad_arriving, grad_potential)


def local_adjoint(grad_normal, normal, totals, hidden_b, weights_b):
    labels = normal.shape[-1]
    inner = jnp.sum(grad_normal * normal, axis=-1, keepdims=True)
    grad_out = (labels / totals * (grad_normal - inner / labels)).astype(jnp.bfloat16)
    grad_weights = jnp.einsum(
        "dxyzk,dxyzl->dkl", hidden_b, grad_out, preferred_element_type=jnp.float32
    )
    grad_hidden = jnp.einsum(
        "dxyzl,dkl->dxyzk", grad_out, weights_b, preferred_element_type=jnp.float32
    )
    return (grad_weights, grad_hidden)


def adjoint_terms(grad_hidden, potential, messages, whole):
    ratios = [grad_hidden[OPPOSE[index]] / messages[index] for index in range(6)]
    total = ratios[0]
    for index in range(1, 6):
        total = total + ratios[index]
    unary_term = whole * total
    scaled = potential * whole
    grad_messages = []
    for edge in range(6):
        partial_sum = None
        for index in range(6):
            if index == edge:
                continue
            partial_sum = ratios[index] if partial_sum is None else partial_sum + ratios[index]
        grad_messages.append((partial_sum * (scaled / messages[edge])).astype(jnp.bfloat16))
    return (unary_term, grad_messages)


def all_sum(value, axes):
    count = 1
    for axis in axes:
        count *= lax.axis_size(axis)
    rows = value.reshape(count, -1)
    mine = jnp.sum(lax.all_to_all(rows, axes, 0, 0, tiled=True), axis=0, keepdims=True)
    spread_out = jnp.broadcast_to(mine, rows.shape)
    return lax.all_to_all(spread_out, axes, 0, 0, tiled=True).reshape(value.shape)


def body(unary, compat, saved_first, saved_second, cotangent):
    potential = jnp.exp(unary.astype(jnp.float32))
    weights = jnp.exp(compat)
    weights_b = weights.astype(jnp.bfloat16)
    lower_edge = (lax.axis_index("gx") == 0, lax.axis_index("gy") == 0, lax.axis_index("gz") == 0)
    upper_edge = (
        lax.axis_index("gx") == lax.axis_size("gx") - 1,
        lax.axis_index("gy") == lax.axis_size("gy") - 1,
        lax.axis_index("gz") == lax.axis_size("gz") - 1,
    )
    first = [saved_first[index].astype(jnp.float32) for index in range(6)]
    second = [saved_second[index].astype(jnp.float32) for index in range(6)]
    whole_two = full_product(second)
    hidden_two, normal_two, totals_two = send_terms(potential, second, whole_two, weights_b)
    arriving = spread(
        [normal_two[index].astype(jnp.bfloat16) for index in range(6)], lower_edge, upper_edge
    )
    arriving = [value.astype(jnp.float32) for value in arriving]
    grad_arriving, grad_potential = belief_adjoint(potential, arriving, cotangent)
    grad_normal_two = gather_back(grad_arriving)
    weights_two, grad_hidden_two = local_adjoint(
        grad_normal_two, normal_two, totals_two, hidden_two, weights_b
    )
    unary_two, grad_second = adjoint_terms(grad_hidden_two, potential, second, whole_two)
    grad_potential = grad_potential + unary_two
    whole_one = full_product(first)
    hidden_one, normal_one, totals_one = send_terms(potential, first, whole_one, weights_b)
    grad_normal_one = gather_back(grad_second)
    weights_one, grad_hidden_one = local_adjoint(
        grad_normal_one, normal_one, totals_one, hidden_one, weights_b
    )
    ratios_one = [grad_hidden_one[OPPOSE[index]] / first[index] for index in range(6)]
    total_one = ratios_one[0]
    for index in range(1, 6):
        total_one = total_one + ratios_one[index]
    grad_potential = grad_potential + whole_one * total_one
    grad_unary = potential * grad_potential
    summed = all_sum(weights_two + weights_one, ("gx", "gy", "gz"))
    grad_compat = weights * summed
    return (grad_unary, grad_compat)


def solution(mesh):
    placed = (
        P("gx", "gy", "gz", None),
        P(),
        P(None, "gx", "gy", "gz", None),
        P(None, "gx", "gy", "gz", None),
        P("gx", "gy", "gz", None),
    )
    return jax.shard_map(
        body,
        mesh=mesh,
        in_specs=placed,
        out_specs=(P("gx", "gy", "gz", None), P()),
        check_vma=False,
    )
```

```python
import jax
import jax.numpy as jnp
from jax import lax
from jax.sharding import PartitionSpec as P

OPPOSE = (1, 0, 3, 2, 5, 4)


def extended(cells, sides, width):
    for axis, dim in sides:
        count = lax.axis_size(axis)
        ends = count - 1
        head = lax.slice_in_dim(cells, 0, width, axis=dim)
        tail = lax.slice_in_dim(cells, cells.shape[dim] - width, cells.shape[dim], axis=dim)
        cells = jnp.concatenate(
            [
                lax.ppermute(tail, axis, [(i, (i + 1) % count) for i in range(ends)]),
                cells,
                lax.ppermute(head, axis, [((i + 1) % count, i) for i in range(ends)]),
            ],
            axis=dim,
        )
    return cells


def full_product(fields):
    result = fields[0]
    for index in range(1, 6):
        result = result * fields[index]
    return result


def send_terms(potential, messages, whole, weights_b):
    labels = potential.shape[-1]
    scaled = potential * whole
    hidden = [scaled / messages[OPPOSE[direction]] for direction in range(6)]
    hidden_b = jnp.stack(hidden).astype(jnp.bfloat16)
    outgoing = jnp.einsum(
        "dxyzk,dkl->dxyzl", hidden_b, weights_b, preferred_element_type=jnp.float32
    )
    totals = jnp.sum(outgoing, axis=-1, keepdims=True)
    normal = labels * outgoing / totals
    return (hidden_b, normal, totals)


def trade(low_face, high_face, axis_dim):
    axis = ("gx", "gy", "gz")[axis_dim]
    count = lax.axis_size(axis)
    odd = lax.axis_index(axis) % 2 == 1
    first = lax.ppermute(
        jnp.where(odd, low_face, high_face), axis, [(i, i ^ 1) for i in range(count)]
    )
    if count > 2:
        second = lax.ppermute(
            jnp.where(odd, high_face, low_face),
            axis,
            [(i, i + 1 if i % 2 == 1 else i - 1) for i in range(1, count - 1)],
        )
    else:
        second = jnp.zeros_like(first)
    lower = jnp.where(odd, first, second)
    upper = jnp.where(odd, second, first)
    return (lower, upper)


def spread(normal_b, lower_edge, upper_edge):
    result = []
    for axis_dim in range(3):
        plus = normal_b[2 * axis_dim]
        minus = normal_b[2 * axis_dim + 1]
        length = plus.shape[axis_dim]
        lower, upper = trade(
            lax.slice_in_dim(minus, 0, 1, axis=axis_dim),
            lax.slice_in_dim(plus, length - 1, length, axis=axis_dim),
            axis_dim,
        )
        ones = jnp.ones_like(lower)
        lower = jnp.where(lower_edge[axis_dim], ones, lower)
        upper = jnp.where(upper_edge[axis_dim], ones, upper)
        result.append(
            jnp.concatenate(
                [lower, lax.slice_in_dim(plus, 0, length - 1, axis=axis_dim)], axis=axis_dim
            )
        )
        result.append(
            jnp.concatenate(
                [lax.slice_in_dim(minus, 1, length, axis=axis_dim), upper], axis=axis_dim
            )
        )
    return result


def gather_back(grad_b):
    result = []
    for axis_dim in range(3):
        plus = grad_b[2 * axis_dim]
        minus = grad_b[2 * axis_dim + 1]
        length = plus.shape[axis_dim]
        lower, upper = trade(
            lax.slice_in_dim(plus, 0, 1, axis=axis_dim),
            lax.slice_in_dim(minus, length - 1, length, axis=axis_dim),
            axis_dim,
        )
        result.append(
            jnp.concatenate(
                [lax.slice_in_dim(plus, 1, length, axis=axis_dim), upper], axis=axis_dim
            )
        )
        result.append(
            jnp.concatenate(
                [lower, lax.slice_in_dim(minus, 0, length - 1, axis=axis_dim)], axis=axis_dim
            )
        )
    return jnp.stack(result).astype(jnp.float32)


def belief_adjoint(potential, arriving, cotangent):
    labels = potential.shape[-1]
    whole = full_product(arriving)
    joint = potential * whole
    summed = jnp.sum(joint, axis=-1, keepdims=True)
    belief = joint / summed
    grad_joint = labels * (cotangent - jnp.sum(cotangent * belief, axis=-1, keepdims=True)) / summed
    grad_potential = grad_joint * whole
    scaled = grad_joint * joint
    grad_arriving = [(scaled / arriving[edge]).astype(jnp.bfloat16) for edge in range(6)]
    return (grad_arriving, grad_potential)


def local_adjoint(grad_normal, normal, totals, hidden_b, weights_b):
    labels = normal.shape[-1]
    inner = jnp.sum(grad_normal * normal, axis=-1, keepdims=True)
    grad_out = (labels / totals * (grad_normal - inner / labels)).astype(jnp.bfloat16)
    grad_weights = jnp.einsum(
        "dxyzk,dxyzl->dkl", hidden_b, grad_out, preferred_element_type=jnp.float32
    )
    grad_hidden = jnp.einsum(
        "dxyzl,dkl->dxyzk", grad_out, weights_b, preferred_element_type=jnp.float32
    )
    return (grad_weights, grad_hidden)


def adjoint_terms(grad_hidden, potential, messages, whole):
    ratios = [grad_hidden[OPPOSE[index]] / messages[index] for index in range(6)]
    total = ratios[0]
    for index in range(1, 6):
        total = total + ratios[index]
    unary_term = whole * total
    scaled = potential * whole
    grad_messages = []
    for edge in range(6):
        partial_sum = None
        for index in range(6):
            if index == edge:
                continue
            partial_sum = ratios[index] if partial_sum is None else partial_sum + ratios[index]
        grad_messages.append((partial_sum * (scaled / messages[edge])).astype(jnp.bfloat16))
    return (unary_term, grad_messages)


def all_sum(value, scale, axes):
    count = 1
    for axis in axes:
        count *= lax.axis_size(axis)
    rows = value.reshape(count, -1)
    mine = jnp.sum(lax.all_to_all(rows, axes, 0, 0, tiled=True), axis=0, keepdims=True)
    own = lax.dynamic_slice_in_dim(scale.reshape(count, -1), lax.axis_index(axes), 1, axis=0)
    spread_out = jnp.broadcast_to(own * mine, rows.shape)
    return lax.all_to_all(spread_out, axes, 0, 0, tiled=True).reshape(value.shape)


def body(unary, compat, saved_first, saved_second, cotangent):
    potential = jnp.exp(unary.astype(jnp.float32))
    weights = jnp.exp(compat)
    weights_b = weights.astype(jnp.bfloat16)
    lower_edge = (lax.axis_index("gx") == 0, lax.axis_index("gy") == 0, lax.axis_index("gz") == 0)
    upper_edge = (
        lax.axis_index("gx") == lax.axis_size("gx") - 1,
        lax.axis_index("gy") == lax.axis_size("gy") - 1,
        lax.axis_index("gz") == lax.axis_size("gz") - 1,
    )
    first = [saved_first[index].astype(jnp.float32) for index in range(6)]
    second = [saved_second[index].astype(jnp.float32) for index in range(6)]
    whole_two = full_product(second)
    hidden_two, normal_two, totals_two = send_terms(potential, second, whole_two, weights_b)
    arriving = spread(
        [normal_two[index].astype(jnp.bfloat16) for index in range(6)], lower_edge, upper_edge
    )
    arriving = [value.astype(jnp.float32) for value in arriving]
    grad_arriving, grad_potential = belief_adjoint(potential, arriving, cotangent)
    grad_normal_two = gather_back(grad_arriving)
    weights_two, grad_hidden_two = local_adjoint(
        grad_normal_two, normal_two, totals_two, hidden_two, weights_b
    )
    unary_two, grad_second = adjoint_terms(grad_hidden_two, potential, second, whole_two)
    grad_potential = grad_potential + unary_two
    whole_one = full_product(first)
    hidden_one, normal_one, totals_one = send_terms(potential, first, whole_one, weights_b)
    grad_normal_one = gather_back(grad_second)
    weights_one, grad_hidden_one = local_adjoint(
        grad_normal_one, normal_one, totals_one, hidden_one, weights_b
    )
    ratios_one = [grad_hidden_one[OPPOSE[index]] / first[index] for index in range(6)]
    total_one = ratios_one[0]
    for index in range(1, 6):
        total_one = total_one + ratios_one[index]
    grad_potential = grad_potential + whole_one * total_one
    grad_unary = potential * grad_potential
    grad_compat = all_sum(weights_two + weights_one, weights, ("gx", "gy", "gz"))
    return (grad_unary, grad_compat)


def solution(mesh):
    placed = (
        P("gx", "gy", "gz", None),
        P(),
        P(None, "gx", "gy", "gz", None),
        P(None, "gx", "gy", "gz", None),
        P("gx", "gy", "gz", None),
    )
    return jax.shard_map(
        body,
        mesh=mesh,
        in_specs=placed,
        out_specs=(P("gx", "gy", "gz", None), P()),
        check_vma=False,
    )
```

```python
import jax
import jax.numpy as jnp
from jax import lax
from jax.sharding import PartitionSpec as P

OPPOSE = (1, 0, 3, 2, 5, 4)


def extended(cells, sides, width):
    for axis, dim in sides:
        count = lax.axis_size(axis)
        ends = count - 1
        head = lax.slice_in_dim(cells, 0, width, axis=dim)
        tail = lax.slice_in_dim(cells, cells.shape[dim] - width, cells.shape[dim], axis=dim)
        cells = jnp.concatenate(
            [
                lax.ppermute(tail, axis, [(i, (i + 1) % count) for i in range(ends)]),
                cells,
                lax.ppermute(head, axis, [((i + 1) % count, i) for i in range(ends)]),
            ],
            axis=dim,
        )
    return cells


def full_product(fields):
    result = fields[0]
    for index in range(1, 6):
        result = result * fields[index]
    return result


def except_products(fields):
    count = len(fields)
    prefix, suffix = [None] * count, [None] * count
    running = None
    for index in range(count):
        prefix[index] = running
        running = fields[index] if running is None else running * fields[index]
    running = None
    for index in reversed(range(count)):
        suffix[index] = running
        running = fields[index] if running is None else running * fields[index]
    result = []
    for index in range(count):
        if prefix[index] is None:
            result.append(suffix[index])
        elif suffix[index] is None:
            result.append(prefix[index])
        else:
            result.append(prefix[index] * suffix[index])
    return result


def send_terms(potential, messages, whole, weights_b):
    labels = potential.shape[-1]
    others = except_products(messages)
    hidden = [potential * others[OPPOSE[direction]] for direction in range(6)]
    hidden_b = jnp.stack(hidden).astype(jnp.bfloat16)
    outgoing = jnp.einsum(
        "dxyzk,dkl->dxyzl", hidden_b, weights_b, preferred_element_type=jnp.float32
    )
    totals = jnp.sum(outgoing, axis=-1, keepdims=True)
    normal = outgoing * (labels / totals)
    return (hidden_b, normal, totals)


def trade(low_face, high_face, axis_dim):
    axis = ("gx", "gy", "gz")[axis_dim]
    count = lax.axis_size(axis)
    odd = lax.axis_index(axis) % 2 == 1
    first = lax.ppermute(
        jnp.where(odd, low_face, high_face), axis, [(i, i ^ 1) for i in range(count)]
    )
    if count > 2:
        second = lax.ppermute(
            jnp.where(odd, high_face, low_face),
            axis,
            [(i, i + 1 if i % 2 == 1 else i - 1) for i in range(1, count - 1)],
        )
    else:
        second = jnp.zeros_like(first)
    lower = jnp.where(odd, first, second)
    upper = jnp.where(odd, second, first)
    return (lower, upper)


def spread(normal_b, lower_edge, upper_edge):
    result = []
    for axis_dim in range(3):
        plus = normal_b[2 * axis_dim]
        minus = normal_b[2 * axis_dim + 1]
        length = plus.shape[axis_dim]
        lower, upper = trade(
            lax.slice_in_dim(minus, 0, 1, axis=axis_dim),
            lax.slice_in_dim(plus, length - 1, length, axis=axis_dim),
            axis_dim,
        )
        ones = jnp.ones_like(lower)
        lower = jnp.where(lower_edge[axis_dim], ones, lower)
        upper = jnp.where(upper_edge[axis_dim], ones, upper)
        result.append(
            jnp.concatenate(
                [lower, lax.slice_in_dim(plus, 0, length - 1, axis=axis_dim)], axis=axis_dim
            )
        )
        result.append(
            jnp.concatenate(
                [lax.slice_in_dim(minus, 1, length, axis=axis_dim), upper], axis=axis_dim
            )
        )
    return result


def gather_back(grad_b):
    result = []
    for axis_dim in range(3):
        plus = grad_b[2 * axis_dim]
        minus = grad_b[2 * axis_dim + 1]
        length = plus.shape[axis_dim]
        lower, upper = trade(
            lax.slice_in_dim(plus, 0, 1, axis=axis_dim),
            lax.slice_in_dim(minus, length - 1, length, axis=axis_dim),
            axis_dim,
        )
        result.append(
            jnp.concatenate(
                [lax.slice_in_dim(plus, 1, length, axis=axis_dim), upper], axis=axis_dim
            )
        )
        result.append(
            jnp.concatenate(
                [lower, lax.slice_in_dim(minus, 0, length - 1, axis=axis_dim)], axis=axis_dim
            )
        )
    return jnp.stack(result).astype(jnp.float32)


def belief_adjoint(potential, arriving, cotangent):
    labels = potential.shape[-1]
    whole = full_product(arriving)
    joint = potential * whole
    summed = jnp.sum(joint, axis=-1, keepdims=True)
    inverse = 1.0 / summed
    belief = joint * inverse
    grad_joint = labels * (cotangent - jnp.sum(cotangent * belief, axis=-1, keepdims=True)) * inverse
    grad_potential = grad_joint * whole
    scaled = grad_joint * potential
    others = except_products(arriving)
    grad_arriving = [(scaled * others[edge]).astype(jnp.bfloat16) for edge in range(6)]
    return (grad_arriving, grad_potential)


def local_adjoint(grad_normal, normal, totals, hidden_b, weights_b):
    labels = normal.shape[-1]
    inner = jnp.sum(grad_normal * normal, axis=-1, keepdims=True)
    grad_out = (labels / totals * (grad_normal - inner / labels)).astype(jnp.bfloat16)
    grad_weights = jnp.einsum(
        "dxyzk,dxyzl->dkl", hidden_b, grad_out, preferred_element_type=jnp.float32
    )
    grad_hidden = jnp.einsum(
        "dxyzl,dkl->dxyzk", grad_out, weights_b, preferred_element_type=jnp.float32
    )
    return (grad_weights, grad_hidden)


def adjoint_terms(grad_hidden, potential, messages, whole):
    ratios = [grad_hidden[OPPOSE[index]] / messages[index] for index in range(6)]
    total = ratios[0]
    for index in range(1, 6):
        total = total + ratios[index]
    unary_term = whole * total
    others = except_products(messages)
    grad_messages = []
    for edge in range(6):
        partial_sum = None
        for index in range(6):
            if index == edge:
                continue
            partial_sum = ratios[index] if partial_sum is None else partial_sum + ratios[index]
        grad_messages.append((partial_sum * (potential * others[edge])).astype(jnp.bfloat16))
    return (unary_term, grad_messages)


def all_sum(value, scale, axes):
    count = 1
    for axis in axes:
        count *= lax.axis_size(axis)
    rows = value.reshape(count, -1)
    mine = jnp.sum(lax.all_to_all(rows, axes, 0, 0, tiled=True), axis=0, keepdims=True)
    own = lax.dynamic_slice_in_dim(scale.reshape(count, -1), lax.axis_index(axes), 1, axis=0)
    spread_out = jnp.broadcast_to(own * mine, rows.shape)
    return lax.all_to_all(spread_out, axes, 0, 0, tiled=True).reshape(value.shape)


def body(unary, compat, saved_first, saved_second, cotangent):
    potential = jnp.exp(unary.astype(jnp.float32))
    weights = jnp.exp(compat)
    weights_b = weights.astype(jnp.bfloat16)
    lower_edge = (lax.axis_index("gx") == 0, lax.axis_index("gy") == 0, lax.axis_index("gz") == 0)
    upper_edge = (
        lax.axis_index("gx") == lax.axis_size("gx") - 1,
        lax.axis_index("gy") == lax.axis_size("gy") - 1,
        lax.axis_index("gz") == lax.axis_size("gz") - 1,
    )
    first = [saved_first[index].astype(jnp.float32) for index in range(6)]
    second = [saved_second[index].astype(jnp.float32) for index in range(6)]
    whole_two = full_product(second)
    hidden_two, normal_two, totals_two = send_terms(potential, second, whole_two, weights_b)
    arriving = spread(
        [normal_two[index].astype(jnp.bfloat16) for index in range(6)], lower_edge, upper_edge
    )
    arriving = [value.astype(jnp.float32) for value in arriving]
    grad_arriving, grad_potential = belief_adjoint(potential, arriving, cotangent)
    grad_normal_two = gather_back(grad_arriving)
    weights_two, grad_hidden_two = local_adjoint(
        grad_normal_two, normal_two, totals_two, hidden_two, weights_b
    )
    unary_two, grad_second = adjoint_terms(grad_hidden_two, potential, second, whole_two)
    grad_potential = grad_potential + unary_two
    whole_one = full_product(first)
    hidden_one, normal_one, totals_one = send_terms(potential, first, whole_one, weights_b)
    grad_normal_one = gather_back(grad_second)
    weights_one, grad_hidden_one = local_adjoint(
        grad_normal_one, normal_one, totals_one, hidden_one, weights_b
    )
    ratios_one = [grad_hidden_one[OPPOSE[index]] / first[index] for index in range(6)]
    total_one = ratios_one[0]
    for index in range(1, 6):
        total_one = total_one + ratios_one[index]
    grad_potential = grad_potential + whole_one * total_one
    grad_unary = potential * grad_potential
    grad_compat = all_sum(weights_two + weights_one, weights, ("gx", "gy", "gz"))
    return (grad_unary, grad_compat)


def solution(mesh):
    placed = (
        P("gx", "gy", "gz", None),
        P(),
        P(None, "gx", "gy", "gz", None),
        P(None, "gx", "gy", "gz", None),
        P("gx", "gy", "gz", None),
    )
    return jax.shard_map(
        body,
        mesh=mesh,
        in_specs=placed,
        out_specs=(P("gx", "gy", "gz", None), P()),
        check_vma=False,
    )
```

```python
import jax
import jax.numpy as jnp
from jax import lax
from jax.sharding import PartitionSpec as P

OPPOSE = (1, 0, 3, 2, 5, 4)


def extended(cells, sides, width):
    for axis, dim in sides:
        count = lax.axis_size(axis)
        ends = count - 1
        head = lax.slice_in_dim(cells, 0, width, axis=dim)
        tail = lax.slice_in_dim(cells, cells.shape[dim] - width, cells.shape[dim], axis=dim)
        cells = jnp.concatenate(
            [
                lax.ppermute(tail, axis, [(i, (i + 1) % count) for i in range(ends)]),
                cells,
                lax.ppermute(head, axis, [((i + 1) % count, i) for i in range(ends)]),
            ],
            axis=dim,
        )
    return cells


def full_product(fields):
    result = fields[0]
    for index in range(1, 6):
        result = result * fields[index]
    return result


def except_products(fields):
    count = len(fields)
    prefix, suffix = [None] * count, [None] * count
    running = None
    for index in range(count):
        prefix[index] = running
        running = fields[index] if running is None else running * fields[index]
    running = None
    for index in reversed(range(count)):
        suffix[index] = running
        running = fields[index] if running is None else running * fields[index]
    result = []
    for index in range(count):
        if prefix[index] is None:
            result.append(suffix[index])
        elif suffix[index] is None:
            result.append(prefix[index])
        else:
            result.append(prefix[index] * suffix[index])
    return result


def send_terms(potential, messages, whole, weights_b):
    labels = potential.shape[-1]
    scaled = potential * whole
    hidden = [scaled / messages[OPPOSE[direction]] for direction in range(6)]
    hidden_b = jnp.stack(hidden).astype(jnp.bfloat16)
    outgoing = jnp.einsum(
        "dxyzk,dkl->dxyzl", hidden_b, weights_b, preferred_element_type=jnp.float32
    )
    totals = jnp.sum(outgoing, axis=-1, keepdims=True)
    normal = outgoing * (labels / totals)
    return (hidden_b, normal, totals)


def trade(low_face, high_face, axis_dim):
    axis = ("gx", "gy", "gz")[axis_dim]
    count = lax.axis_size(axis)
    odd = lax.axis_index(axis) % 2 == 1
    first = lax.ppermute(
        jnp.where(odd, low_face, high_face), axis, [(i, i ^ 1) for i in range(count)]
    )
    if count > 2:
        second = lax.ppermute(
            jnp.where(odd, high_face, low_face),
            axis,
            [(i, i + 1 if i % 2 == 1 else i - 1) for i in range(1, count - 1)],
        )
    else:
        second = jnp.zeros_like(first)
    lower = jnp.where(odd, first, second)
    upper = jnp.where(odd, second, first)
    return (lower, upper)


def spread(normal_b, lower_edge, upper_edge):
    result = []
    for axis_dim in range(3):
        plus = normal_b[2 * axis_dim]
        minus = normal_b[2 * axis_dim + 1]
        length = plus.shape[axis_dim]
        lower, upper = trade(
            lax.slice_in_dim(minus, 0, 1, axis=axis_dim),
            lax.slice_in_dim(plus, length - 1, length, axis=axis_dim),
            axis_dim,
        )
        ones = jnp.ones_like(lower)
        lower = jnp.where(lower_edge[axis_dim], ones, lower)
        upper = jnp.where(upper_edge[axis_dim], ones, upper)
        result.append(
            jnp.concatenate(
                [lower, lax.slice_in_dim(plus, 0, length - 1, axis=axis_dim)], axis=axis_dim
            )
        )
        result.append(
            jnp.concatenate(
                [lax.slice_in_dim(minus, 1, length, axis=axis_dim), upper], axis=axis_dim
            )
        )
    return result


def gather_back(grad_b):
    result = []
    for axis_dim in range(3):
        plus = grad_b[2 * axis_dim]
        minus = grad_b[2 * axis_dim + 1]
        length = plus.shape[axis_dim]
        lower, upper = trade(
            lax.slice_in_dim(plus, 0, 1, axis=axis_dim),
            lax.slice_in_dim(minus, length - 1, length, axis=axis_dim),
            axis_dim,
        )
        result.append(
            jnp.concatenate(
                [lax.slice_in_dim(plus, 1, length, axis=axis_dim), upper], axis=axis_dim
            )
        )
        result.append(
            jnp.concatenate(
                [lower, lax.slice_in_dim(minus, 0, length - 1, axis=axis_dim)], axis=axis_dim
            )
        )
    return jnp.stack(result).astype(jnp.float32)


def belief_adjoint(potential, arriving, cotangent):
    labels = potential.shape[-1]
    whole = full_product(arriving)
    joint = potential * whole
    summed = jnp.sum(joint, axis=-1, keepdims=True)
    inverse = 1.0 / summed
    belief = joint * inverse
    grad_joint = labels * (cotangent - jnp.sum(cotangent * belief, axis=-1, keepdims=True)) * inverse
    grad_potential = grad_joint * whole
    scaled = grad_joint * potential
    others = except_products(arriving)
    grad_arriving = [(scaled * others[edge]).astype(jnp.bfloat16) for edge in range(6)]
    return (grad_arriving, grad_potential)


def local_adjoint(grad_normal, normal, totals, hidden_b, weights_b):
    labels = normal.shape[-1]
    inner = jnp.sum(grad_normal * normal, axis=-1, keepdims=True)
    grad_out = (labels / totals * (grad_normal - inner / labels)).astype(jnp.bfloat16)
    grad_weights = jnp.einsum(
        "dxyzk,dxyzl->dkl", hidden_b, grad_out, preferred_element_type=jnp.float32
    )
    grad_hidden = jnp.einsum(
        "dxyzl,dkl->dxyzk", grad_out, weights_b, preferred_element_type=jnp.float32
    )
    return (grad_weights, grad_hidden)


def adjoint_terms(grad_hidden, potential, messages, whole):
    ratios = [grad_hidden[OPPOSE[index]] / messages[index] for index in range(6)]
    total = ratios[0]
    for index in range(1, 6):
        total = total + ratios[index]
    unary_term = whole * total
    scaled = potential * whole
    grad_messages = []
    for edge in range(6):
        partial_sum = None
        for index in range(6):
            if index == edge:
                continue
            partial_sum = ratios[index] if partial_sum is None else partial_sum + ratios[index]
        grad_messages.append((partial_sum * (scaled / messages[edge])).astype(jnp.bfloat16))
    return (unary_term, grad_messages)


def all_sum(value, scale, axes):
    count = 1
    for axis in axes:
        count *= lax.axis_size(axis)
    rows = value.reshape(count, -1)
    mine = jnp.sum(lax.all_to_all(rows, axes, 0, 0, tiled=True), axis=0, keepdims=True)
    own = lax.dynamic_slice_in_dim(scale.reshape(count, -1), lax.axis_index(axes), 1, axis=0)
    spread_out = jnp.broadcast_to(own * mine, rows.shape)
    return lax.all_to_all(spread_out, axes, 0, 0, tiled=True).reshape(value.shape)


def body(unary, compat, saved_first, saved_second, cotangent):
    potential = jnp.exp(unary.astype(jnp.float32))
    weights = jnp.exp(compat)
    weights_b = weights.astype(jnp.bfloat16)
    lower_edge = (lax.axis_index("gx") == 0, lax.axis_index("gy") == 0, lax.axis_index("gz") == 0)
    upper_edge = (
        lax.axis_index("gx") == lax.axis_size("gx") - 1,
        lax.axis_index("gy") == lax.axis_size("gy") - 1,
        lax.axis_index("gz") == lax.axis_size("gz") - 1,
    )
    first = [saved_first[index].astype(jnp.float32) for index in range(6)]
    second = [saved_second[index].astype(jnp.float32) for index in range(6)]
    whole_two = full_product(second)
    hidden_two, normal_two, totals_two = send_terms(potential, second, whole_two, weights_b)
    arriving = spread(
        [normal_two[index].astype(jnp.bfloat16) for index in range(6)], lower_edge, upper_edge
    )
    arriving = [value.astype(jnp.float32) for value in arriving]
    grad_arriving, grad_potential = belief_adjoint(potential, arriving, cotangent)
    grad_normal_two = gather_back(grad_arriving)
    weights_two, grad_hidden_two = local_adjoint(
        grad_normal_two, normal_two, totals_two, hidden_two, weights_b
    )
    unary_two, grad_second = adjoint_terms(grad_hidden_two, potential, second, whole_two)
    grad_potential = grad_potential + unary_two
    whole_one = full_product(first)
    hidden_one, normal_one, totals_one = send_terms(potential, first, whole_one, weights_b)
    grad_normal_one = gather_back(grad_second)
    weights_one, grad_hidden_one = local_adjoint(
        grad_normal_one, normal_one, totals_one, hidden_one, weights_b
    )
    ratios_one = [grad_hidden_one[OPPOSE[index]] / first[index] for index in range(6)]
    total_one = ratios_one[0]
    for index in range(1, 6):
        total_one = total_one + ratios_one[index]
    grad_potential = grad_potential + whole_one * total_one
    grad_unary = potential * grad_potential
    grad_compat = all_sum(weights_two + weights_one, weights, ("gx", "gy", "gz"))
    return (grad_unary, grad_compat)


def solution(mesh):
    placed = (
        P("gx", "gy", "gz", None),
        P(),
        P(None, "gx", "gy", "gz", None),
        P(None, "gx", "gy", "gz", None),
        P("gx", "gy", "gz", None),
    )
    return jax.shard_map(
        body,
        mesh=mesh,
        in_specs=placed,
        out_specs=(P("gx", "gy", "gz", None), P()),
        check_vma=False,
    )
```

```python
import jax
import jax.numpy as jnp
from jax import lax
from jax.sharding import PartitionSpec as P

OPPOSE = (1, 0, 3, 2, 5, 4)


def extended(cells, sides, width):
    for axis, dim in sides:
        count = lax.axis_size(axis)
        ends = count - 1
        head = lax.slice_in_dim(cells, 0, width, axis=dim)
        tail = lax.slice_in_dim(cells, cells.shape[dim] - width, cells.shape[dim], axis=dim)
        cells = jnp.concatenate(
            [
                lax.ppermute(tail, axis, [(i, (i + 1) % count) for i in range(ends)]),
                cells,
                lax.ppermute(head, axis, [((i + 1) % count, i) for i in range(ends)]),
            ],
            axis=dim,
        )
    return cells


def full_product(fields):
    result = fields[0]
    for index in range(1, 6):
        result = result * fields[index]
    return result


def except_products(fields):
    count = len(fields)
    prefix, suffix = [None] * count, [None] * count
    running = None
    for index in range(count):
        prefix[index] = running
        running = fields[index] if running is None else running * fields[index]
    running = None
    for index in reversed(range(count)):
        suffix[index] = running
        running = fields[index] if running is None else running * fields[index]
    result = []
    for index in range(count):
        if prefix[index] is None:
            result.append(suffix[index])
        elif suffix[index] is None:
            result.append(prefix[index])
        else:
            result.append(prefix[index] * suffix[index])
    return result


def send_terms(potential, messages, whole, weights_b):
    labels = potential.shape[-1]
    scaled = potential * whole
    hidden = [scaled / messages[OPPOSE[direction]] for direction in range(6)]
    hidden_b = jnp.stack(hidden).astype(jnp.bfloat16)
    outgoing = jnp.einsum(
        "dxyzk,dkl->dxyzl", hidden_b, weights_b, preferred_element_type=jnp.float32
    )
    totals = jnp.sum(outgoing, axis=-1, keepdims=True)
    normal = outgoing * (labels / totals)
    return (hidden_b, normal, totals)


def trade(low_face, high_face, axis_dim):
    axis = ("gx", "gy", "gz")[axis_dim]
    count = lax.axis_size(axis)
    odd = lax.axis_index(axis) % 2 == 1
    first = lax.ppermute(
        jnp.where(odd, low_face, high_face), axis, [(i, i ^ 1) for i in range(count)]
    )
    if count > 2:
        second = lax.ppermute(
            jnp.where(odd, high_face, low_face),
            axis,
            [(i, i + 1 if i % 2 == 1 else i - 1) for i in range(1, count - 1)],
        )
    else:
        second = jnp.zeros_like(first)
    lower = jnp.where(odd, first, second)
    upper = jnp.where(odd, second, first)
    return (lower, upper)


def spread(normal_b, lower_edge, upper_edge):
    result = []
    for axis_dim in range(3):
        plus = normal_b[2 * axis_dim]
        minus = normal_b[2 * axis_dim + 1]
        length = plus.shape[axis_dim]
        lower, upper = trade(
            lax.slice_in_dim(minus, 0, 1, axis=axis_dim),
            lax.slice_in_dim(plus, length - 1, length, axis=axis_dim),
            axis_dim,
        )
        ones = jnp.ones_like(lower)
        lower = jnp.where(lower_edge[axis_dim], ones, lower)
        upper = jnp.where(upper_edge[axis_dim], ones, upper)
        result.append(
            jnp.concatenate(
                [lower, lax.slice_in_dim(plus, 0, length - 1, axis=axis_dim)], axis=axis_dim
            )
        )
        result.append(
            jnp.concatenate(
                [lax.slice_in_dim(minus, 1, length, axis=axis_dim), upper], axis=axis_dim
            )
        )
    return result


def gather_back(grad_b):
    result = []
    for axis_dim in range(3):
        plus = grad_b[2 * axis_dim]
        minus = grad_b[2 * axis_dim + 1]
        length = plus.shape[axis_dim]
        lower, upper = trade(
            lax.slice_in_dim(plus, 0, 1, axis=axis_dim),
            lax.slice_in_dim(minus, length - 1, length, axis=axis_dim),
            axis_dim,
        )
        result.append(
            jnp.concatenate(
                [lax.slice_in_dim(plus, 1, length, axis=axis_dim), upper], axis=axis_dim
            )
        )
        result.append(
            jnp.concatenate(
                [lower, lax.slice_in_dim(minus, 0, length - 1, axis=axis_dim)], axis=axis_dim
            )
        )
    return jnp.stack(result).astype(jnp.float32)


def belief_adjoint(potential, arriving, cotangent):
    labels = potential.shape[-1]
    whole = full_product(arriving)
    joint = potential * whole
    summed = jnp.sum(joint, axis=-1, keepdims=True)
    inverse = 1.0 / summed
    belief = joint * inverse
    grad_joint = labels * (cotangent - jnp.sum(cotangent * belief, axis=-1, keepdims=True)) * inverse
    grad_potential = grad_joint * whole
    scaled = grad_joint * potential
    others = except_products(arriving)
    grad_arriving = [(scaled * others[edge]).astype(jnp.bfloat16) for edge in range(6)]
    return (grad_arriving, grad_potential)


def local_adjoint(grad_normal, normal, totals, hidden_b, weights_b):
    labels = normal.shape[-1]
    inner = jnp.sum(grad_normal * normal, axis=-1, keepdims=True)
    grad_out = (labels / totals * (grad_normal - inner / labels)).astype(jnp.bfloat16)
    grad_weights = jnp.einsum(
        "dxyzk,dxyzl->dkl", hidden_b, grad_out, preferred_element_type=jnp.float32
    )
    grad_hidden = jnp.einsum(
        "dxyzl,dkl->dxyzk", grad_out, weights_b, preferred_element_type=jnp.float32
    )
    return (grad_weights, grad_hidden)


def adjoint_terms(grad_hidden, potential, messages, whole):
    inverses = [1.0 / messages[index] for index in range(6)]
    ratios = [grad_hidden[OPPOSE[index]] * inverses[index] for index in range(6)]
    total = ratios[0]
    for index in range(1, 6):
        total = total + ratios[index]
    unary_term = whole * total
    scaled = potential * whole
    grad_messages = []
    for edge in range(6):
        partial_sum = None
        for index in range(6):
            if index == edge:
                continue
            partial_sum = ratios[index] if partial_sum is None else partial_sum + ratios[index]
        grad_messages.append((partial_sum * (scaled * inverses[edge])).astype(jnp.bfloat16))
    return (unary_term, grad_messages)


def all_sum(value, scale, axes):
    count = 1
    for axis in axes:
        count *= lax.axis_size(axis)
    rows = value.reshape(count, -1)
    mine = jnp.sum(lax.all_to_all(rows, axes, 0, 0, tiled=True), axis=0, keepdims=True)
    own = lax.dynamic_slice_in_dim(scale.reshape(count, -1), lax.axis_index(axes), 1, axis=0)
    spread_out = jnp.broadcast_to(own * mine, rows.shape)
    return lax.all_to_all(spread_out, axes, 0, 0, tiled=True).reshape(value.shape)


def body(unary, compat, saved_first, saved_second, cotangent):
    potential = jnp.exp(unary.astype(jnp.float32))
    weights = jnp.exp(compat)
    weights_b = weights.astype(jnp.bfloat16)
    lower_edge = (lax.axis_index("gx") == 0, lax.axis_index("gy") == 0, lax.axis_index("gz") == 0)
    upper_edge = (
        lax.axis_index("gx") == lax.axis_size("gx") - 1,
        lax.axis_index("gy") == lax.axis_size("gy") - 1,
        lax.axis_index("gz") == lax.axis_size("gz") - 1,
    )
    first = [saved_first[index].astype(jnp.float32) for index in range(6)]
    second = [saved_second[index].astype(jnp.float32) for index in range(6)]
    whole_two = full_product(second)
    hidden_two, normal_two, totals_two = send_terms(potential, second, whole_two, weights_b)
    arriving = spread(
        [normal_two[index].astype(jnp.bfloat16) for index in range(6)], lower_edge, upper_edge
    )
    arriving = [value.astype(jnp.float32) for value in arriving]
    grad_arriving, grad_potential = belief_adjoint(potential, arriving, cotangent)
    grad_normal_two = gather_back(grad_arriving)
    weights_two, grad_hidden_two = local_adjoint(
        grad_normal_two, normal_two, totals_two, hidden_two, weights_b
    )
    unary_two, grad_second = adjoint_terms(grad_hidden_two, potential, second, whole_two)
    grad_potential = grad_potential + unary_two
    whole_one = full_product(first)
    hidden_one, normal_one, totals_one = send_terms(potential, first, whole_one, weights_b)
    grad_normal_one = gather_back(grad_second)
    weights_one, grad_hidden_one = local_adjoint(
        grad_normal_one, normal_one, totals_one, hidden_one, weights_b
    )
    ratios_one = [grad_hidden_one[OPPOSE[index]] / first[index] for index in range(6)]
    total_one = ratios_one[0]
    for index in range(1, 6):
        total_one = total_one + ratios_one[index]
    grad_potential = grad_potential + whole_one * total_one
    grad_unary = potential * grad_potential
    grad_compat = all_sum(weights_two + weights_one, weights, ("gx", "gy", "gz"))
    return (grad_unary, grad_compat)


def solution(mesh):
    placed = (
        P("gx", "gy", "gz", None),
        P(),
        P(None, "gx", "gy", "gz", None),
        P(None, "gx", "gy", "gz", None),
        P("gx", "gy", "gz", None),
    )
    return jax.shard_map(
        body,
        mesh=mesh,
        in_specs=placed,
        out_specs=(P("gx", "gy", "gz", None), P()),
        check_vma=False,
    )
```

```python
import jax
import jax.numpy as jnp
from jax import lax
from jax.sharding import PartitionSpec as P

OPPOSE = (1, 0, 3, 2, 5, 4)


def extended(cells, sides, width):
    for axis, dim in sides:
        count = lax.axis_size(axis)
        ends = count - 1
        head = lax.slice_in_dim(cells, 0, width, axis=dim)
        tail = lax.slice_in_dim(cells, cells.shape[dim] - width, cells.shape[dim], axis=dim)
        cells = jnp.concatenate(
            [
                lax.ppermute(tail, axis, [(i, (i + 1) % count) for i in range(ends)]),
                cells,
                lax.ppermute(head, axis, [((i + 1) % count, i) for i in range(ends)]),
            ],
            axis=dim,
        )
    return cells


def full_product(fields):
    result = fields[0]
    for index in range(1, 6):
        result = result * fields[index]
    return result


def except_products(fields):
    count = len(fields)
    prefix, suffix = [None] * count, [None] * count
    running = None
    for index in range(count):
        prefix[index] = running
        running = fields[index] if running is None else running * fields[index]
    running = None
    for index in reversed(range(count)):
        suffix[index] = running
        running = fields[index] if running is None else running * fields[index]
    result = []
    for index in range(count):
        if prefix[index] is None:
            result.append(suffix[index])
        elif suffix[index] is None:
            result.append(prefix[index])
        else:
            result.append(prefix[index] * suffix[index])
    return result


def send_terms(potential, messages, whole, weights_b):
    labels = potential.shape[-1]
    scaled = potential * whole
    hidden = [scaled / messages[OPPOSE[direction]] for direction in range(6)]
    hidden_b = jnp.stack(hidden).astype(jnp.bfloat16)
    outgoing = jnp.einsum(
        "dxyzk,dkl->dxyzl", hidden_b, weights_b, preferred_element_type=jnp.float32
    )
    totals = jnp.sum(outgoing, axis=-1, keepdims=True)
    normal = outgoing * (labels / totals)
    return (hidden_b, normal, totals)


def trade(low_face, high_face, axis_dim):
    axis = ("gx", "gy", "gz")[axis_dim]
    count = lax.axis_size(axis)
    odd = lax.axis_index(axis) % 2 == 1
    first = lax.ppermute(
        jnp.where(odd, low_face, high_face), axis, [(i, i ^ 1) for i in range(count)]
    )
    if count > 2:
        second = lax.ppermute(
            jnp.where(odd, high_face, low_face),
            axis,
            [(i, i + 1 if i % 2 == 1 else i - 1) for i in range(1, count - 1)],
        )
    else:
        second = jnp.zeros_like(first)
    lower = jnp.where(odd, first, second)
    upper = jnp.where(odd, second, first)
    return (lower, upper)


def spread(normal_b, lower_edge, upper_edge):
    result = []
    for axis_dim in range(3):
        plus = normal_b[2 * axis_dim]
        minus = normal_b[2 * axis_dim + 1]
        length = plus.shape[axis_dim]
        lower, upper = trade(
            lax.slice_in_dim(minus, 0, 1, axis=axis_dim),
            lax.slice_in_dim(plus, length - 1, length, axis=axis_dim),
            axis_dim,
        )
        ones = jnp.ones_like(lower)
        lower = jnp.where(lower_edge[axis_dim], ones, lower)
        upper = jnp.where(upper_edge[axis_dim], ones, upper)
        result.append(
            jnp.concatenate(
                [lower, lax.slice_in_dim(plus, 0, length - 1, axis=axis_dim)], axis=axis_dim
            )
        )
        result.append(
            jnp.concatenate(
                [lax.slice_in_dim(minus, 1, length, axis=axis_dim), upper], axis=axis_dim
            )
        )
    return result


def gather_back(grad_b):
    result = []
    for axis_dim in range(3):
        plus = grad_b[2 * axis_dim]
        minus = grad_b[2 * axis_dim + 1]
        length = plus.shape[axis_dim]
        lower, upper = trade(
            lax.slice_in_dim(plus, 0, 1, axis=axis_dim),
            lax.slice_in_dim(minus, length - 1, length, axis=axis_dim),
            axis_dim,
        )
        result.append(
            jnp.concatenate(
                [lax.slice_in_dim(plus, 1, length, axis=axis_dim), upper], axis=axis_dim
            )
        )
        result.append(
            jnp.concatenate(
                [lower, lax.slice_in_dim(minus, 0, length - 1, axis=axis_dim)], axis=axis_dim
            )
        )
    return jnp.stack(result).astype(jnp.float32)


def belief_adjoint(potential, arriving, cotangent):
    labels = potential.shape[-1]
    whole = full_product(arriving)
    joint = potential * whole
    summed = jnp.sum(joint, axis=-1, keepdims=True)
    inverse = 1.0 / summed
    belief = joint * inverse
    grad_joint = labels * (cotangent - jnp.sum(cotangent * belief, axis=-1, keepdims=True)) * inverse
    grad_potential = grad_joint * whole
    scaled = grad_joint * potential
    others = except_products(arriving)
    grad_arriving = [(scaled * others[edge]).astype(jnp.bfloat16) for edge in range(6)]
    return (grad_arriving, grad_potential)


def local_adjoint(grad_normal, normal, totals, hidden_b, weights_b):
    labels = normal.shape[-1]
    outgoing = jnp.einsum(
        "dxyzk,dkl->dxyzl",
        lax.optimization_barrier(hidden_b),
        weights_b,
        preferred_element_type=jnp.float32,
    )
    normal = outgoing * (labels / totals)
    inner = jnp.sum(grad_normal * normal, axis=-1, keepdims=True)
    grad_out = (labels / totals * (grad_normal - inner / labels)).astype(jnp.bfloat16)
    grad_weights = jnp.einsum(
        "dxyzk,dxyzl->dkl", hidden_b, grad_out, preferred_element_type=jnp.float32
    )
    grad_hidden = jnp.einsum(
        "dxyzl,dkl->dxyzk", grad_out, weights_b, preferred_element_type=jnp.float32
    )
    return (grad_weights, grad_hidden)


def adjoint_terms(grad_hidden, potential, messages, whole):
    inverses = [1.0 / messages[index] for index in range(6)]
    ratios = [grad_hidden[OPPOSE[index]] * inverses[index] for index in range(6)]
    total = ratios[0]
    for index in range(1, 6):
        total = total + ratios[index]
    unary_term = whole * total
    scaled = potential * whole
    grad_messages = []
    for edge in range(6):
        partial_sum = None
        for index in range(6):
            if index == edge:
                continue
            partial_sum = ratios[index] if partial_sum is None else partial_sum + ratios[index]
        grad_messages.append((partial_sum * (scaled * inverses[edge])).astype(jnp.bfloat16))
    return (unary_term, grad_messages)


def all_sum(value, scale, axes):
    count = 1
    for axis in axes:
        count *= lax.axis_size(axis)
    rows = value.reshape(count, -1)
    mine = jnp.sum(lax.all_to_all(rows, axes, 0, 0, tiled=True), axis=0, keepdims=True)
    own = lax.dynamic_slice_in_dim(scale.reshape(count, -1), lax.axis_index(axes), 1, axis=0)
    spread_out = jnp.broadcast_to(own * mine, rows.shape)
    return lax.all_to_all(spread_out, axes, 0, 0, tiled=True).reshape(value.shape)


def body(unary, compat, saved_first, saved_second, cotangent):
    potential = jnp.exp(unary.astype(jnp.float32))
    weights = jnp.exp(compat)
    weights_b = weights.astype(jnp.bfloat16)
    lower_edge = (lax.axis_index("gx") == 0, lax.axis_index("gy") == 0, lax.axis_index("gz") == 0)
    upper_edge = (
        lax.axis_index("gx") == lax.axis_size("gx") - 1,
        lax.axis_index("gy") == lax.axis_size("gy") - 1,
        lax.axis_index("gz") == lax.axis_size("gz") - 1,
    )
    first = [saved_first[index].astype(jnp.float32) for index in range(6)]
    second = [saved_second[index].astype(jnp.float32) for index in range(6)]
    whole_two = full_product(second)
    hidden_two, normal_two, totals_two = send_terms(potential, second, whole_two, weights_b)
    arriving = spread(
        [normal_two[index].astype(jnp.bfloat16) for index in range(6)], lower_edge, upper_edge
    )
    arriving = [value.astype(jnp.float32) for value in arriving]
    grad_arriving, grad_potential = belief_adjoint(potential, arriving, cotangent)
    grad_normal_two = gather_back(grad_arriving)
    weights_two, grad_hidden_two = local_adjoint(
        grad_normal_two, normal_two, totals_two, hidden_two, weights_b
    )
    unary_two, grad_second = adjoint_terms(grad_hidden_two, potential, second, whole_two)
    grad_potential = grad_potential + unary_two
    whole_one = full_product(first)
    hidden_one, normal_one, totals_one = send_terms(potential, first, whole_one, weights_b)
    grad_normal_one = gather_back(grad_second)
    weights_one, grad_hidden_one = local_adjoint(
        grad_normal_one, normal_one, totals_one, hidden_one, weights_b
    )
    ratios_one = [grad_hidden_one[OPPOSE[index]] / first[index] for index in range(6)]
    total_one = ratios_one[0]
    for index in range(1, 6):
        total_one = total_one + ratios_one[index]
    grad_potential = grad_potential + whole_one * total_one
    grad_unary = potential * grad_potential
    grad_compat = all_sum(weights_two + weights_one, weights, ("gx", "gy", "gz"))
    return (grad_unary, grad_compat)


def solution(mesh):
    placed = (
        P("gx", "gy", "gz", None),
        P(),
        P(None, "gx", "gy", "gz", None),
        P(None, "gx", "gy", "gz", None),
        P("gx", "gy", "gz", None),
    )
    return jax.shard_map(
        body,
        mesh=mesh,
        in_specs=placed,
        out_specs=(P("gx", "gy", "gz", None), P()),
        check_vma=False,
    )
```

```python
import jax
import jax.numpy as jnp
from jax import lax
from jax.sharding import PartitionSpec as P

OPPOSE = (1, 0, 3, 2, 5, 4)


def extended(cells, sides, width):
    for axis, dim in sides:
        count = lax.axis_size(axis)
        ends = count - 1
        head = lax.slice_in_dim(cells, 0, width, axis=dim)
        tail = lax.slice_in_dim(cells, cells.shape[dim] - width, cells.shape[dim], axis=dim)
        cells = jnp.concatenate(
            [
                lax.ppermute(tail, axis, [(i, (i + 1) % count) for i in range(ends)]),
                cells,
                lax.ppermute(head, axis, [((i + 1) % count, i) for i in range(ends)]),
            ],
            axis=dim,
        )
    return cells


def full_product(fields):
    result = fields[0]
    for index in range(1, 6):
        result = result * fields[index]
    return result


def except_products(fields):
    count = len(fields)
    prefix, suffix = [None] * count, [None] * count
    running = None
    for index in range(count):
        prefix[index] = running
        running = fields[index] if running is None else running * fields[index]
    running = None
    for index in reversed(range(count)):
        suffix[index] = running
        running = fields[index] if running is None else running * fields[index]
    result = []
    for index in range(count):
        if prefix[index] is None:
            result.append(suffix[index])
        elif suffix[index] is None:
            result.append(prefix[index])
        else:
            result.append(prefix[index] * suffix[index])
    return result


def send_terms(potential, messages, whole, weights_b):
    labels = potential.shape[-1]
    scaled = potential * whole
    hidden = [scaled / messages[OPPOSE[direction]] for direction in range(6)]
    hidden_b = jnp.stack(hidden).astype(jnp.bfloat16)
    outgoing = jnp.einsum(
        "dxyzk,dkl->dxyzl", hidden_b, weights_b, preferred_element_type=jnp.float32
    )
    totals = jnp.sum(outgoing, axis=-1, keepdims=True)
    normal = outgoing * (labels / totals)
    return (hidden_b, normal, totals)


def trade(low_face, high_face, axis_dim):
    axis = ("gx", "gy", "gz")[axis_dim]
    count = lax.axis_size(axis)
    odd = lax.axis_index(axis) % 2 == 1
    first = lax.ppermute(
        jnp.where(odd, low_face, high_face), axis, [(i, i ^ 1) for i in range(count)]
    )
    if count > 2:
        second = lax.ppermute(
            jnp.where(odd, high_face, low_face),
            axis,
            [(i, i + 1 if i % 2 == 1 else i - 1) for i in range(1, count - 1)],
        )
    else:
        second = jnp.zeros_like(first)
    lower = jnp.where(odd, first, second)
    upper = jnp.where(odd, second, first)
    return (lower, upper)


def spread(normal_b, lower_edge, upper_edge):
    result = []
    for axis_dim in range(3):
        plus = normal_b[2 * axis_dim]
        minus = normal_b[2 * axis_dim + 1]
        length = plus.shape[axis_dim]
        lower, upper = trade(
            lax.slice_in_dim(minus, 0, 1, axis=axis_dim),
            lax.slice_in_dim(plus, length - 1, length, axis=axis_dim),
            axis_dim,
        )
        ones = jnp.ones_like(lower)
        lower = jnp.where(lower_edge[axis_dim], ones, lower)
        upper = jnp.where(upper_edge[axis_dim], ones, upper)
        result.append(
            jnp.concatenate(
                [lower, lax.slice_in_dim(plus, 0, length - 1, axis=axis_dim)], axis=axis_dim
            )
        )
        result.append(
            jnp.concatenate(
                [lax.slice_in_dim(minus, 1, length, axis=axis_dim), upper], axis=axis_dim
            )
        )
    return result


def gather_back(grad_b):
    result = []
    for axis_dim in range(3):
        plus = grad_b[2 * axis_dim]
        minus = grad_b[2 * axis_dim + 1]
        length = plus.shape[axis_dim]
        lower, upper = trade(
            lax.slice_in_dim(plus, 0, 1, axis=axis_dim),
            lax.slice_in_dim(minus, length - 1, length, axis=axis_dim),
            axis_dim,
        )
        result.append(
            jnp.concatenate(
                [lax.slice_in_dim(plus, 1, length, axis=axis_dim), upper], axis=axis_dim
            )
        )
        result.append(
            jnp.concatenate(
                [lower, lax.slice_in_dim(minus, 0, length - 1, axis=axis_dim)], axis=axis_dim
            )
        )
    return jnp.stack(result).astype(jnp.float32)


def belief_adjoint(potential, arriving, cotangent):
    labels = potential.shape[-1]
    whole = full_product(arriving)
    joint = potential * whole
    summed = jnp.sum(joint, axis=-1, keepdims=True)
    inverse = 1.0 / summed
    belief = joint * inverse
    grad_joint = labels * (cotangent - jnp.sum(cotangent * belief, axis=-1, keepdims=True)) * inverse
    grad_potential = grad_joint * whole
    scaled = grad_joint * potential
    others = except_products(arriving)
    grad_arriving = [(scaled * others[edge]).astype(jnp.bfloat16) for edge in range(6)]
    return (grad_arriving, grad_potential)


def local_adjoint(grad_normal, normal, totals, hidden_b, weights_b):
    labels = normal.shape[-1]
    inner = jnp.sum(grad_normal * normal, axis=-1, keepdims=True)
    grad_out = (labels / totals * (grad_normal - inner / labels)).astype(jnp.bfloat16)
    grad_weights = jnp.einsum(
        "dxyzk,dxyzl->dkl", hidden_b, grad_out, preferred_element_type=jnp.float32
    )
    grad_hidden = jnp.einsum(
        "dxyzl,dkl->dxyzk", grad_out, weights_b, preferred_element_type=jnp.float32
    )
    return (grad_weights, grad_hidden)


def adjoint_terms(grad_hidden, potential, messages, whole):
    inverses = [1.0 / messages[index] for index in range(6)]
    ratios = [grad_hidden[OPPOSE[index]] * inverses[index] for index in range(6)]
    total = ratios[0]
    for index in range(1, 6):
        total = total + ratios[index]
    unary_term = whole * total
    scaled = potential * whole
    grad_messages = []
    for edge in range(6):
        partial_sum = None
        for index in range(6):
            if index == edge:
                continue
            partial_sum = ratios[index] if partial_sum is None else partial_sum + ratios[index]
        grad_messages.append((partial_sum * (scaled * inverses[edge])).astype(jnp.bfloat16))
    return (unary_term, grad_messages)


def all_sum(value, scale, axes):
    count = 1
    for axis in axes:
        count *= lax.axis_size(axis)
    rows = value.reshape(count, -1)
    mine = jnp.sum(lax.all_to_all(rows, axes, 0, 0, tiled=True), axis=0, keepdims=True)
    own = lax.dynamic_slice_in_dim(scale.reshape(count, -1), lax.axis_index(axes), 1, axis=0)
    spread_out = jnp.broadcast_to(own * mine, rows.shape)
    return lax.all_to_all(spread_out, axes, 0, 0, tiled=True).reshape(value.shape)


def body(unary, compat, saved_first, saved_second, cotangent):
    potential = jnp.exp(unary.astype(jnp.float32))
    weights = jnp.exp(compat)
    weights_b = weights.astype(jnp.bfloat16)
    lower_edge = (lax.axis_index("gx") == 0, lax.axis_index("gy") == 0, lax.axis_index("gz") == 0)
    upper_edge = (
        lax.axis_index("gx") == lax.axis_size("gx") - 1,
        lax.axis_index("gy") == lax.axis_size("gy") - 1,
        lax.axis_index("gz") == lax.axis_size("gz") - 1,
    )
    first = [saved_first[index].astype(jnp.float32) for index in range(6)]
    second = [saved_second[index].astype(jnp.float32) for index in range(6)]
    whole_two = full_product(second)
    hidden_two, normal_two, totals_two = send_terms(potential, second, whole_two, weights_b)
    arriving = spread(
        [normal_two[index].astype(jnp.bfloat16) for index in range(6)], lower_edge, upper_edge
    )
    arriving = [value.astype(jnp.float32) for value in arriving]
    grad_arriving, grad_potential = belief_adjoint(potential, arriving, cotangent)
    grad_normal_two = gather_back(grad_arriving)
    weights_two, grad_hidden_two = local_adjoint(
        grad_normal_two, normal_two, totals_two, hidden_two, weights_b
    )
    unary_two, grad_second = adjoint_terms(grad_hidden_two, potential, second, whole_two)
    grad_potential = grad_potential + unary_two
    whole_one = full_product(first)
    hidden_one, normal_one, totals_one = send_terms(potential, first, whole_one, weights_b)
    grad_normal_one = gather_back(grad_second)
    weights_one, grad_hidden_one = local_adjoint(
        grad_normal_one, normal_one, totals_one, hidden_one, weights_b
    )
    others_one = except_products(first)
    total_one = grad_hidden_one[OPPOSE[0]] * others_one[0]
    for index in range(1, 6):
        total_one = total_one + grad_hidden_one[OPPOSE[index]] * others_one[index]
    grad_potential = grad_potential + total_one
    grad_unary = potential * grad_potential
    grad_compat = all_sum(weights_two + weights_one, weights, ("gx", "gy", "gz"))
    return (grad_unary, grad_compat)


def solution(mesh):
    placed = (
        P("gx", "gy", "gz", None),
        P(),
        P(None, "gx", "gy", "gz", None),
        P(None, "gx", "gy", "gz", None),
        P("gx", "gy", "gz", None),
    )
    return jax.shard_map(
        body,
        mesh=mesh,
        in_specs=placed,
        out_specs=(P("gx", "gy", "gz", None), P()),
        check_vma=False,
    )
```
